32 devices in a mesh: group: 2 (over y), tm: 16 (over z, x, core).
Axes of the slice: x: 2, y: 2, z: 4, core: 2. Of those that a mesh axis runs over, the one named last changes fastest.
Arguments:
- features: bfloat16 [64, 192, 8, 256], P(('group', 'tm')), parts along dimension 0, may hold values from -6 to 6
- video_frames: int32 [16], P('group'), parts along dimension 0, may hold values from 1 to 16, 32 in all
- gain_first: float32 [192], replicated, may hold values from 0.1 to 1.9
- conv_first: bfloat16 [3, 3, 3, 192, 192], replicated, may hold values from -0.078125 to 0.078125
- gain_second: float32 [192], replicated, may hold values from 0.1 to 1.9
- conv_second: bfloat16 [3, 3, 3, 192, 192], replicated, may hold values from -0.078125 to 0.078125
Outputs:
- block_out: bfloat16 [64, 192, 8, 256], P(('group', 'tm')), parts along dimension 0
The draws below stay inside these ranges and needn't reach their ends.
There are 2 independent parts, one for each index of `group`. The reference program is written for one: setup_inputs(seed, part) draws one part's arguments, and reference() takes and returns one part's arrays. A program takes and returns all parts, laid end to end along the dimension named above; an argument that names none is the same for every part. Nothing has to cross between parts.
Inputs may be any that keep to these rules, and one draw needn't show every extreme that they name: `video_frames`: each video's frame count; they sum to 32 and the largest is exactly 16.
All inputs are finite; a program needn't handle non-finite values.
Results may differ from the reference program's by a relative error of at most 0.0039.
Values may be sent and summed in bfloat16 or wider, within the bound.
No kernel may reach another device: no remote copies, remote signals or barrier semaphores. Data moves between devices by JAX's collectives and lax.ppermute only.
A program may use at most 128 MiB of HBM per device.

```python
import math
import jax
import jax.numpy as jnp
import numpy as np
from jax import lax

C = 192
ROWS = 8
COLS = 256
FRAMES = 32
VIDEOS = 8
MOST = 16


def block_levels(rng, dims, cuts, least, top_value):
    def one(axis_at, parts):
        heights = jax.random.uniform(jax.random.fold_in(jax.random.fold_in(rng, 6), axis_at), (parts,), jnp.float32, least / len(cuts), top_value / len(cuts))
        return jnp.repeat(jnp.exp(heights), dims[axis_at] // parts).reshape((-1,) + (1,) * (len(dims) - axis_at - 1))

    loudness = one(*cuts[0])
    for cut in cuts[1:]:
        loudness = loudness * one(*cut)
    return loudness


def profile(count, total, reach, slope):
    weights = [(1 << 20) // math.isqrt(rank ** slope) + 1 for rank in range(2, count + 1)]
    spare, counts = total - reach - (count - 1), [1] * (count - 1)
    while spare > 0:
        movable = [i for i in range(count - 1) if counts[i] < reach]
        whole, left = sum([weights[i] for i in movable]), spare
        for i in movable:
            extra = min(reach - counts[i], max(1, left * weights[i] // whole), spare)
            counts[i] = counts[i] + extra
            spare = spare - extra
    return np.array([reach] + counts)


def uneven_parts(key, number_of, total, most, slope):
    if number_of == 2:
        one = jax.random.randint(key, (), max(1, total - most), min(most, total - 1) + 1)
        return jnp.stack([one, total - one])
    tallies = jnp.asarray(profile(number_of, total, most, slope), jnp.int32)
    couples = (number_of - 1) // 2
    giver, taker = tallies[1:1 + 2 * couples:2], tallies[2:2 + 2 * couples:2]
    slack = jnp.minimum(giver - 1, most - taker)
    moved = jax.random.randint(jax.random.fold_in(key, 1), (couples,), 0, 1 << 20) % (slack + 1)
    tallies = tallies.at[1:1 + 2 * couples:2].set(giver - moved).at[2:2 + 2 * couples:2].set(taker + moved)
    return tallies[jax.random.permutation(jax.random.fold_in(key, 2), number_of)]


def centred(stream_key, extent, deviation, bound, split=(), kind=jnp.bfloat16):
    values = deviation * jax.random.normal(stream_key, extent, jnp.float32)
    if split:
        values = values * block_levels(stream_key, extent, split, -0.22, 0.18)
    return jnp.clip(values, -bound, bound).astype(kind)


def setup_inputs(seed: int = 0, part: int = 0) -> dict:
    keys = jax.random.split(jax.random.key(seed), 7)
    own_keys = jax.random.split(jax.random.fold_in(keys[6], part), 7)
    return {
        "features": centred(own_keys[0], (FRAMES, C, ROWS, COLS), 1.0, 6.0, ((0, 16),)),
        "video_frames": uneven_parts(own_keys[1], VIDEOS, FRAMES, MOST, 2).astype(jnp.int32),
        "gain_first": jnp.clip(1.0 + 0.18 * jax.random.normal(keys[2], (C,), jnp.float32), 0.1, 1.9),
        "conv_first": centred(keys[3], (3, 3, 3, C, C), (27 * C) ** -0.5, 0.078125),
        "gain_second": jnp.clip(1.0 + 0.18 * jax.random.normal(keys[4], (C,), jnp.float32), 0.1, 1.9),
        "conv_second": centred(keys[5], (3, 3, 3, C, C), (27 * C) ** -0.5, 0.078125),
    }


def video_start(video_frames, positions):
    video_ends = jnp.cumsum(video_frames).astype(jnp.int32)
    video_begins = (video_ends - video_frames).astype(jnp.int32)
    inside = video_begins[None, :] <= positions[:, None]
    return lax.optimization_barrier(jnp.max(jnp.where(inside, video_begins[None, :], 0), axis=1)).astype(jnp.int32)

def build_masks(video_frames, positions):
    starts = video_start(video_frames, positions)
    columns = [(positions - lag_tap >= starts).astype(jnp.float32) for lag_tap in range(3)]
    return jnp.stack(columns, axis=1)

def normalize(values, gain):
    mean_square = lax.optimization_barrier(jnp.mean(values * values, axis=1, keepdims=True))
    return values * lax.rsqrt(mean_square + 1e-06) * gain.astype(jnp.float32)[None, :, None, None]

def activate(values, gain):
    return jax.nn.silu(normalize(values, gain)).astype(jnp.bfloat16)

def causal_conv(padded, weights, masks):
    out_frames = padded.shape[0] - 2
    summed = None
    for lag_tap in range(3):
        frames = lax.slice_in_dim(padded, 2 - lag_tap, 2 - lag_tap + out_frames, axis=0)
        tapped = lax.conv_general_dilated(frames, weights[lag_tap], (1, 1), ((1, 1), (1, 1)), dimension_numbers=('NCHW', 'HWIO', 'NCHW'), preferred_element_type=jnp.float32)
        tapped = masks[:, lag_tap][:, None, None, None] * tapped
        summed = tapped if summed is None else summed + tapped
    return summed

def reference(features, video_frames, gain_first, conv_first, gain_second, conv_second):
    positions = jnp.arange(features.shape[0], dtype=jnp.int32)
    masks = build_masks(video_frames, positions)
    first_act = activate(features.astype(jnp.float32), gain_first)
    zero_pad = jnp.zeros((2,) + first_act.shape[1:], jnp.bfloat16)
    first_out = causal_conv(jnp.concatenate([zero_pad, first_act], axis=0), conv_first, masks)
    second_act = activate(first_out, gain_second)
    second_out = causal_conv(jnp.concatenate([zero_pad, second_act], axis=0), conv_second, masks)
    return (features.astype(jnp.float32) + second_out).astype(jnp.bfloat16)
```

```python
import functools

import jax
import jax.numpy as jnp
from jax import lax
from jax.experimental import pallas as pl
from jax.experimental.pallas import tpu as pltpu
from jax.sharding import PartitionSpec as P


def shifted(value, axis, steps):
    count = lax.axis_size(axis)
    initial, last = (max(0, -steps), min(count, count - steps))
    return lax.ppermute(value, axis, [(source, source + steps) for source in range(initial, last)])


def video_start(video_frames, positions):
    video_ends = jnp.cumsum(video_frames)
    video_begins = video_ends - video_frames
    inside = video_begins[None, :] <= positions[:, None]
    return jnp.max(jnp.where(inside, video_begins[None, :], 0), axis=1)


def build_masks(video_frames, positions):
    starts = video_start(video_frames, positions)
    columns = [(positions - lag_tap >= starts).astype(jnp.int32) for lag_tap in range(3)]
    return jnp.stack(columns, axis=1)


def silu_norm(values, gain):
    mean_square = jnp.mean(values * values, axis=0, keepdims=True)
    normed = values * lax.rsqrt(mean_square + 1e-06) * gain
    return normed / (1.0 + jnp.exp(-normed))


def conv_kernel(mask_ref, edge_ref, act_ref, w_ref, aux_ref, out_ref, stack_ref, *, cols, second):
    frames, chans, pixels = act_ref.shape
    rows = pixels // cols
    lane = lax.broadcasted_iota(jnp.int32, (chans, pixels), 1) % cols
    zeros = jnp.zeros((3 * chans, cols), jnp.bfloat16)
    for source in range(frames + 2):
        stack_ref[source, :, 0:cols] = zeros
        stack_ref[source, :, cols + pixels : 2 * cols + pixels] = zeros
        x = edge_ref[source] if source < 2 else act_ref[source - 2]
        xf = x.astype(jnp.float32)
        left = jnp.where(lane == 0, 0.0, pltpu.roll(xf, 1, 1))
        right = jnp.where(lane == cols - 1, 0.0, pltpu.roll(xf, pixels - 1, 1))
        stack_ref[source, 0:chans, cols : cols + pixels] = left.astype(jnp.bfloat16)
        stack_ref[source, chans : 2 * chans, cols : cols + pixels] = x
        stack_ref[source, 2 * chans : 3 * chans, cols : cols + pixels] = right.astype(jnp.bfloat16)

    for frame in range(frames):

        def row_body(row, carry, frame=frame):
            start = pl.multiple_of(row * cols, cols)

            def tap(lag, acc):
                for dr in range(3):
                    rhs = stack_ref[frame + 2 - lag, :, pl.ds(start + dr * cols, cols)]
                    part = jnp.dot(w_ref[lag, dr], rhs, preferred_element_type=jnp.float32)
                    acc = part if acc is None else acc + part
                return acc

            acc = tap(0, None)
            for lag in (1, 2):
                acc = lax.cond(mask_ref[frame, lag] != 0, functools.partial(tap, lag), lambda a: a, acc)
            if second:
                res = aux_ref[frame, :, pl.ds(start, cols)].astype(jnp.float32)
                out_ref[frame, :, pl.ds(start, cols)] = (res + acc).astype(out_ref.dtype)
            else:
                out_ref[frame, :, pl.ds(start, cols)] = silu_norm(acc, aux_ref[...]).astype(out_ref.dtype)
            return carry

        lax.fori_loop(0, rows, row_body, 0)


def causal_conv(masks, edge, act, weights, aux, cols, second):
    frames, chans, pixels = act.shape
    wt = jnp.transpose(weights, (0, 1, 4, 2, 3)).reshape(3, 3, chans, 3 * chans)
    full = lambda shape: pl.BlockSpec(shape, lambda i, m: (0,) * len(shape))
    grid_spec = pltpu.PrefetchScalarGridSpec(
        num_scalar_prefetch=1,
        grid=(1,),
        in_specs=[full(edge.shape), full(act.shape), full(wt.shape), full(aux.shape)],
        out_specs=full(act.shape),
        scratch_shapes=[pltpu.VMEM((frames + 2, 3 * chans, pixels + 2 * cols), jnp.bfloat16)],
    )
    return pl.pallas_call(
        functools.partial(conv_kernel, cols=cols, second=second),
        grid_spec=grid_spec,
        out_shape=jax.ShapeDtypeStruct(act.shape, jnp.bfloat16),
        compiler_params=pltpu.CompilerParams(vmem_limit_bytes=60 * 1024 * 1024),
    )(masks, edge, act, wt, aux)


def per_device(features, video_frames, gain_first, conv_first, gain_second, conv_second):
    frames, chans, rows, cols = features.shape
    offset = lax.axis_index("tm") * frames
    positions = offset + jnp.arange(frames, dtype=jnp.int32)
    masks = build_masks(video_frames, positions)
    flat = features.reshape(frames, chans, rows * cols)
    xf = flat.astype(jnp.float32)
    mean_square = jnp.mean(xf * xf, axis=1, keepdims=True)
    normed = xf * lax.rsqrt(mean_square + 1e-06) * gain_first[None, :, None]
    first_act = (normed / (1.0 + jnp.exp(-normed))).astype(jnp.bfloat16)
    edge_first = shifted(first_act[frames - 2 :], "tm", 1)
    second_act = causal_conv(masks, edge_first, first_act, conv_first, gain_second[:, None], cols, False)
    edge_second = shifted(second_act[frames - 2 :], "tm", 1)
    out = causal_conv(masks, edge_second, second_act, conv_second, flat, cols, True)
    return out.reshape(frames, chans, rows, cols)


def solution(mesh):
    in_specs = (P(("group", "tm"), None, None, None), P("group"), P(), P(), P(), P())
    out_specs = P(("group", "tm"), None, None, None)
    return jax.shard_map(
        per_device, mesh=mesh, in_specs=in_specs, out_specs=out_specs, check_vma=False
    )
```
